256 devices in a mesh: section: 4 (over x), rows: 16 (over z_lo, y, core), dp: 4 (over z_hi).
Axes of the slice: x: 4, y: 4, z: 8 (z_hi: 4, z_lo: 2; z = z_hi * 2 + z_lo), core: 2. Of those that a mesh axis runs over, the one named last changes fastest.
Arguments:
- latent: bfloat16 [8, 2, 64, 8, 192], P('dp', None, 'rows'), may hold values from -6 to 6
- enc_weight: bfloat16 [4, 5184, 192], P('section'), may hold values from -0.078125 to 0.078125
- dec_weight: bfloat16 [4, 5184, 192], P('section'), may hold values from -0.078125 to 0.078125
- enc_gain: float32 [4, 192], P('section'), may hold values from 0.1 to 1.9
- dec_gain: float32 [4, 192], P('section'), may hold values from 0.1 to 1.9
- out_grad: bfloat16 [8, 2, 64, 8, 192], P('dp', None, 'rows'), may hold values from -6 to 6
Outputs:
- enc_wgrad: float32 [4, 5184, 192], P('section', ('rows', 'dp'))
- dec_wgrad: float32 [4, 5184, 192], P('section', ('rows', 'dp'))
- enc_ggrad: float32 [4, 192], P('section', ('rows', 'dp'))
- dec_ggrad: float32 [4, 192], P('section', ('rows', 'dp'))
The draws below stay inside these ranges and needn't reach their ends.
All inputs are finite; a program needn't handle non-finite values.
Results may differ from the reference program's by a relative error of at most 0.028.
Values may be sent and summed in bfloat16 or wider, within the bound.
No kernel may reach another device: no remote copies, remote signals or barrier semaphores. Data moves between devices by JAX's collectives and lax.ppermute only.
A program may use at most 128 MiB of HBM per device.

```python
import math
import jax
import jax.numpy as jnp
from jax import lax

C = 192
GROUPS = 32
KC = 5184
FR = 2
COLS = 8
HALF = 4
HH = 64
BATCH = 8


def draw_latent(key, part):
    position = jnp.arange(HH, dtype=jnp.float32) / max(HH - 1, 1)
    amplitude = 0.7 * jnp.exp2(position)
    base_vals = jnp.clip(jax.random.normal(key, (BATCH, FR, HH, COLS, C), jnp.float32), -4.0, 4.0)
    return (base_vals * amplitude[None, None, :, None, None]).astype(jnp.bfloat16)


def shard_levels(rng, extent, cuts, least, top_value):
    level = 1.0
    for axis_at, shards_of in cuts:
        draws = jax.random.uniform(jax.random.fold_in(jax.random.fold_in(rng, 6), axis_at), (shards_of,), jnp.float32, least / len(cuts), top_value / len(cuts))
        level = level * jnp.repeat(jnp.exp(draws), extent[axis_at] // shards_of).reshape((-1,) + (1,) * (len(extent) - 1 - axis_at))
    return level


def gaussian(stream_key, extent, scale, most, split=(), held_as=jnp.bfloat16):
    values = jax.random.normal(stream_key, extent, jnp.float32) * scale
    if len(split) > 0:
        values = shard_levels(stream_key, extent, split, -0.22, 0.18) * values
    return jnp.clip(values, min=-most, max=most).astype(held_as)


def setup_inputs(seed: int = 0) -> dict:
    key_list = jax.random.split(jax.random.key(seed), 7)
    return {
        "latent": draw_latent(jax.random.fold_in(key_list[6], 71), 0),
        "enc_weight": gaussian(key_list[1], (HALF, KC, C), KC ** -0.5, 0.078125, ((0, 4),)),
        "dec_weight": gaussian(key_list[2], (HALF, KC, C), KC ** -0.5, 0.078125, ((0, 4),)),
        "enc_gain": jnp.clip(1.0 + 0.18 * jax.random.normal(key_list[3], (HALF, C), jnp.float32), 0.1, 1.9),
        "dec_gain": jnp.clip(1.0 + 0.18 * jax.random.normal(key_list[4], (HALF, C), jnp.float32), 0.1, 1.9),
        "out_grad": gaussian(key_list[5], (BATCH, FR, HH, COLS, C), 1.0, 6.0, ((0, 4), (2, 16))),
    }


EPSILON = 1e-05

def gather_patches(grown_rows):
    frames, padded_rows, columns, channels = grown_rows.shape
    inner_rows = padded_rows - 2
    padded = jnp.pad(grown_rows, ((1, 1), (0, 0), (1, 1), (0, 0)))
    pieces = []
    for lag_frame in range(3):
        for lag_row in range(3):
            for lag_column in range(3):
                pieces.append(padded[lag_frame:lag_frame + frames, lag_row:lag_row + inner_rows, lag_column:lag_column + columns, :])
    return jnp.concatenate(pieces, axis=-1).reshape(frames * inner_rows * columns, 27 * channels)

def convolve(volume, weights):

    def single(sample):
        grown_rows = jnp.pad(sample, ((0, 0), (1, 1), (0, 0), (0, 0)))
        flat_out = jnp.dot(gather_patches(grown_rows), weights, preferred_element_type=jnp.float32)
        return flat_out.reshape(sample.shape[:-1] + (weights.shape[1],))
    return lax.map(single, volume)

def weight_gradient(volume, cotangent):

    def single(summed, paired):
        sample, grad_low = paired
        grown_rows = jnp.pad(sample, ((0, 0), (1, 1), (0, 0), (0, 0)))
        patches = gather_patches(grown_rows)
        product = lax.dot_general(patches, grad_low.reshape(-1, grad_low.shape[-1]), (((0,), (0,)), ((), ())), preferred_element_type=jnp.float32)
        return (summed + product, None)
    initial = jnp.zeros((27 * volume.shape[-1], cotangent.shape[-1]), jnp.float32)
    summed, unused = lax.scan(single, initial, (volume, cotangent))
    return summed

def group_stats(volume):
    batches = volume.shape[0]
    channels = volume.shape[-1]
    grouped = volume.reshape(batches, -1, GROUPS, channels // GROUPS)
    counted = grouped.shape[1] * grouped.shape[3]
    centre = lax.optimization_barrier(jnp.sum(grouped, axis=(1, 3))) / counted
    deviation = grouped - centre[:, None, :, None]
    spread = lax.optimization_barrier(jnp.sum(deviation * deviation, axis=(1, 3))) / counted
    return (centre, lax.rsqrt(spread + EPSILON))

def per_channel(values, channels):
    return jnp.repeat(values, channels // GROUPS, axis=-1)[:, None, None, None, :]

def forward_block(volume, gain_vec, weights):
    channels = volume.shape[-1]
    centre, inverse = group_stats(volume)
    normed = (volume - per_channel(centre, channels)) * per_channel(inverse, channels)
    active = jax.nn.silu(normed * gain_vec).astype(jnp.bfloat16)
    return (active, volume + convolve(active, weights))

def backward_block(volume, gain_vec, weights, active, cotangent):
    channels = volume.shape[-1]
    batches = volume.shape[0]
    centre, inverse = group_stats(volume)
    inverse_full = per_channel(inverse, channels)
    normed = (volume - per_channel(centre, channels)) * inverse_full
    zvalue = normed * gain_vec
    cotangent_low = cotangent.astype(jnp.bfloat16)
    blocks = weights.reshape(27, channels, -1)[::-1]
    reverse_weights = jnp.swapaxes(blocks, 1, 2).reshape(-1, channels)
    act_grad = convolve(cotangent_low, reverse_weights)
    logistic = jax.nn.sigmoid(zvalue)
    pre_grad = act_grad * logistic * (1.0 + zvalue * (1.0 - logistic))
    hat_grad = pre_grad * gain_vec
    grouped_grad = hat_grad.reshape(batches, -1, GROUPS, channels // GROUPS)
    grouped_hat = normed.reshape(batches, -1, GROUPS, channels // GROUPS)
    counted = grouped_grad.shape[1] * grouped_grad.shape[3]
    first_sum = lax.optimization_barrier(jnp.sum(grouped_grad, axis=(1, 3)))
    second_sum = lax.optimization_barrier(jnp.sum(grouped_grad * grouped_hat, axis=(1, 3)))
    input_grad = inverse_full * (hat_grad - per_channel(first_sum / counted, channels) - normed * per_channel(second_sum / counted, channels))
    gain_grad = lax.optimization_barrier(jnp.sum(pre_grad * normed, axis=(0, 1, 2, 3)))
    return (cotangent + input_grad, weight_gradient(active, cotangent_low), gain_grad)

def reference(latent, enc_weight, dec_weight, enc_gain, dec_gain, out_grad):
    hidden = latent
    enc_inputs = []
    enc_active = []
    for level_idx in range(HALF):
        enc_inputs.append(hidden)
        active, result = forward_block(hidden.astype(jnp.float32), enc_gain[level_idx], enc_weight[level_idx])
        enc_active.append(active)
        hidden = result.astype(jnp.bfloat16)
    dec_downs = [None] * HALF
    dec_active = [None] * HALF
    coming = hidden
    for level_idx in reversed(range(HALF)):
        dec_downs[level_idx] = coming
        united = coming.astype(jnp.float32) + enc_inputs[level_idx].astype(jnp.float32)
        active, result = forward_block(united, dec_gain[level_idx], dec_weight[level_idx])
        dec_active[level_idx] = active
        coming = result.astype(jnp.bfloat16)
    loss_scale = 1.0 / math.sqrt(BATCH * FR * HH * COLS)
    cotangent = out_grad.astype(jnp.float32) * loss_scale
    skip_grads = [None] * HALF
    dec_weights_grad = [None] * HALF
    dec_gains_grad = [None] * HALF
    for level_idx in range(HALF):
        united = dec_downs[level_idx].astype(jnp.float32) + enc_inputs[level_idx].astype(jnp.float32)
        cotangent, weight_grad, gain_grad = backward_block(united, dec_gain[level_idx], dec_weight[level_idx], dec_active[level_idx], cotangent)
        skip_grads[level_idx] = cotangent
        dec_weights_grad[level_idx] = weight_grad
        dec_gains_grad[level_idx] = gain_grad
    enc_weights_grad = [None] * HALF
    enc_gains_grad = [None] * HALF
    for level_idx in reversed(range(HALF)):
        passed, weight_grad, gain_grad = backward_block(enc_inputs[level_idx].astype(jnp.float32), enc_gain[level_idx], enc_weight[level_idx], enc_active[level_idx], cotangent)
        cotangent = passed + skip_grads[level_idx]
        enc_weights_grad[level_idx] = weight_grad
        enc_gains_grad[level_idx] = gain_grad
    return (jnp.stack(enc_weights_grad), jnp.stack(dec_weights_grad), jnp.stack(enc_gains_grad), jnp.stack(dec_gains_grad))
```

```python
import math

import jax
import jax.numpy as jnp
from jax import lax
from jax.sharding import PartitionSpec as P

GROUPS = 32


EPSILON = 1e-05


def spread_groups(values, channels):
    return jnp.repeat(values, channels // GROUPS, axis=-1)[:, None, None, None, :]


def rows_allsum(value):
    count = lax.axis_size("rows")
    if count & (count - 1):
        return lax.psum(value, "rows")
    mask = 1
    while mask < count:
        partner = [(i, i ^ mask) for i in range(count)]
        value = value + lax.ppermute(value, "rows", partner)
        mask *= 2
    return value


def rows_gather(value):
    count = lax.axis_size("rows")
    slots = jnp.zeros((count,) + value.shape, value.dtype)
    slots = lax.dynamic_update_index_in_dim(slots, value, lax.axis_index("rows"), 0)
    return rows_allsum(slots)


def edge_rows(block):
    count = lax.axis_size("rows")
    up = [(i, i + 1) for i in range(count - 1)]
    down = [(i + 1, i) for i in range(count - 1)]
    low = lax.ppermute(block[:, :, -1:], "rows", up)
    high = lax.ppermute(block[:, :, :1], "rows", down)
    return low, high


def gather_patches(grown_rows):
    frames, padded_rows, columns, channels = grown_rows.shape
    inner_rows = padded_rows - 2
    padded = jnp.pad(grown_rows, ((1, 1), (0, 0), (1, 1), (0, 0)))
    pieces = []
    for lag_frame in range(3):
        for lag_row in range(3):
            for lag_column in range(3):
                pieces.append(
                    padded[
                        lag_frame : lag_frame + frames,
                        lag_row : lag_row + inner_rows,
                        lag_column : lag_column + columns,
                        :,
                    ]
                )
    return jnp.concatenate(pieces, axis=-1).reshape(frames * inner_rows * columns, 27 * channels)


def conv_rows(grown, weights):
    batches, frames, grown_rows, columns, _ = grown.shape
    patches = jax.vmap(gather_patches)(grown).reshape(-1, weights.shape[0])
    out = jnp.dot(patches, weights, preferred_element_type=jnp.float32)
    return out.reshape(batches, frames, grown_rows - 2, columns, weights.shape[1])


def flipped(weights):
    channels = weights.shape[1]
    blocks = weights.reshape(27, -1, channels)[::-1]
    return jnp.swapaxes(blocks, 1, 2).reshape(-1, blocks.shape[1])


def with_halo(low, own, high, keep_low, keep_high):
    low = jnp.where(keep_low, low, jnp.zeros_like(low))
    high = jnp.where(keep_high, high, jnp.zeros_like(high))
    return jnp.concatenate([low, own, high], axis=2)


def forward_block(volume, gain_vec, weights, counted, keep_low, keep_high):
    batches = volume.shape[0]
    channels = volume.shape[-1]
    local_count = counted // lax.axis_size("rows")
    grouped = volume.reshape(batches, -1, GROUPS, channels // GROUPS)
    local_sum = jnp.sum(grouped, axis=(1, 3))
    local_mean = local_sum / local_count
    deviation = grouped - local_mean[:, None, :, None]
    local_sq = jnp.sum(deviation * deviation, axis=(1, 3))
    low, high = edge_rows(volume)
    gathered = rows_gather(jnp.stack([local_sum, local_sq]))
    sums = gathered[:, 0]
    squares = gathered[:, 1]
    centre = jnp.sum(sums, axis=0) / counted
    part_means = sums / local_count
    spread = (
        jnp.sum(squares, axis=0) + local_count * jnp.sum((part_means - centre) ** 2, axis=0)
    ) / counted
    inverse = lax.rsqrt(spread + EPSILON)
    full = jnp.concatenate([low, volume, high], axis=2)
    normed = (full - spread_groups(centre, channels)) * spread_groups(inverse, channels)
    active = jax.nn.silu(normed * gain_vec).astype(jnp.bfloat16)
    active = with_halo(active[:, :, :1], active[:, :, 1:-1], active[:, :, -1:], keep_low, keep_high)
    result = volume + conv_rows(active, weights)
    return active, centre, inverse, result


def backward_block(volume, gain_vec, reverse_weights, centre, inverse, cot, counted, keep_low, keep_high):
    channels = volume.shape[-1]
    batches = volume.shape[0]
    inverse_full = spread_groups(inverse, channels)
    normed = (volume - spread_groups(centre, channels)) * inverse_full
    zvalue = normed * gain_vec
    cot_low = cot.astype(jnp.bfloat16)
    act_grad = conv_rows(cot_low, reverse_weights)
    logistic = jax.nn.sigmoid(zvalue)
    pre_grad = act_grad * logistic * (1.0 + zvalue * (1.0 - logistic))
    hat_grad = pre_grad * gain_vec
    grouped_grad = hat_grad.reshape(batches, -1, GROUPS, channels // GROUPS)
    grouped_hat = normed.reshape(batches, -1, GROUPS, channels // GROUPS)
    halo_low, halo_high = edge_rows(jnp.concatenate([hat_grad, normed], axis=-1))
    sums = rows_allsum(
        jnp.stack([jnp.sum(grouped_grad, axis=(1, 3)), jnp.sum(grouped_grad * grouped_hat, axis=(1, 3))])
    )
    first = spread_groups(sums[0] / counted, channels)
    second = spread_groups(sums[1] / counted, channels)
    grad_full = jnp.concatenate([halo_low[..., :channels], hat_grad, halo_high[..., :channels]], axis=2)
    hat_full = jnp.concatenate([halo_low[..., channels:], normed, halo_high[..., channels:]], axis=2)
    passed = cot + inverse_full * (grad_full - first - hat_full * second)
    passed = with_halo(passed[:, :, :1], passed[:, :, 1:-1], passed[:, :, -1:], keep_low, keep_high)
    gain_part = jnp.sum((pre_grad * normed).reshape(-1, channels), axis=0)
    return passed, cot_low[:, :, 1:-1], gain_part


def weight_gradient(grown, cot_low):
    patches = jax.vmap(gather_patches)(grown)
    patches = patches.reshape(-1, patches.shape[-1])
    flat_cot = cot_low.reshape(-1, cot_low.shape[-1])
    return lax.dot_general(
        patches, flat_cot, (((0,), (0,)), ((), ())), preferred_element_type=jnp.float32
    )


def on_device(latent, enc_weight, dec_weight, enc_gain, dec_gain, out_grad):
    section_pos = lax.axis_index("section")
    rows_pos = lax.axis_index("rows")
    keep_low = rows_pos > 0
    keep_high = rows_pos < lax.axis_size("rows") - 1
    batches, frames, rows_here, columns, channels = latent.shape
    levels = lax.axis_size("section")
    counted = frames * rows_here * columns * (channels // GROUPS) * lax.axis_size("rows")
    cells_all = batches * lax.axis_size("dp") * frames * rows_here * lax.axis_size("rows") * columns
    loss_scale = 1.0 / math.sqrt(cells_all)
    enc_all = lax.all_gather(enc_weight[0], "section")
    dec_all = lax.all_gather(dec_weight[0], "section")
    enc_gains = lax.all_gather(enc_gain[0], "section")
    dec_gains = lax.all_gather(dec_gain[0], "section")

    hidden = latent.astype(jnp.float32)
    enc_inputs = []
    enc_active = []
    enc_stats = []
    for level in range(levels):
        enc_inputs.append(hidden)
        active, centre, inverse, result = forward_block(
            hidden, enc_gains[level], enc_all[level], counted, keep_low, keep_high
        )
        enc_active.append(active)
        enc_stats.append((centre, inverse))
        hidden = result.astype(jnp.bfloat16).astype(jnp.float32)
    dec_inputs = [None] * levels
    dec_active = [None] * levels
    dec_stats = [None] * levels
    coming = hidden
    for level in reversed(range(levels)):
        united = coming + enc_inputs[level]
        dec_inputs[level] = united
        active, centre, inverse, result = forward_block(
            united, dec_gains[level], dec_all[level], counted, keep_low, keep_high
        )
        dec_active[level] = active
        dec_stats[level] = (centre, inverse)
        coming = result.astype(jnp.bfloat16).astype(jnp.float32)

    seeded_low, seeded_high = edge_rows(out_grad)
    cot = with_halo(seeded_low, out_grad, seeded_high, keep_low, keep_high).astype(jnp.float32) * loss_scale
    skip_grads = [None] * levels
    dec_cots = [None] * levels
    dec_gain_parts = [None] * levels
    for level in range(levels):
        cot, cot_low, gain_part = backward_block(
            dec_inputs[level],
            dec_gains[level],
            flipped(dec_all[level]),
            dec_stats[level][0],
            dec_stats[level][1],
            cot,
            counted,
            keep_low,
            keep_high,
        )
        skip_grads[level] = cot
        dec_cots[level] = cot_low
        dec_gain_parts[level] = gain_part
    own_dec = weight_gradient(
        lax.dynamic_index_in_dim(jnp.stack(dec_active), section_pos, 0, keepdims=False),
        lax.dynamic_index_in_dim(jnp.stack(dec_cots), section_pos, 0, keepdims=False),
    )
    dec_result = lax.psum_scatter(own_dec, ("rows", "dp"), scatter_dimension=0, tiled=True)
    dec_gain_own = lax.dynamic_index_in_dim(jnp.stack(dec_gain_parts), section_pos, 0, keepdims=False)

    enc_cots = [None] * levels
    enc_gain_parts = [None] * levels
    for level in reversed(range(levels)):
        passed, cot_low, gain_part = backward_block(
            enc_inputs[level],
            enc_gains[level],
            flipped(enc_all[level]),
            enc_stats[level][0],
            enc_stats[level][1],
            cot,
            counted,
            keep_low,
            keep_high,
        )
        cot = passed + skip_grads[level]
        enc_cots[level] = cot_low
        enc_gain_parts[level] = gain_part
    own_enc = weight_gradient(
        lax.dynamic_index_in_dim(jnp.stack(enc_active), section_pos, 0, keepdims=False),
        lax.dynamic_index_in_dim(jnp.stack(enc_cots), section_pos, 0, keepdims=False),
    )
    enc_result = lax.psum_scatter(own_enc, ("rows", "dp"), scatter_dimension=0, tiled=True)
    enc_gain_own = lax.dynamic_index_in_dim(jnp.stack(enc_gain_parts), section_pos, 0, keepdims=False)
    gain_all = lax.psum_scatter(
        jnp.stack([enc_gain_own, dec_gain_own]), ("rows", "dp"), scatter_dimension=1, tiled=True
    )
    return (enc_result[None], dec_result[None], gain_all[0:1], gain_all[1:2])


def solution(mesh):
    in_specs = (
        P("dp", None, "rows", None, None),
        P("section", None, None),
        P("section", None, None),
        P("section", None),
        P("section", None),
        P("dp", None, "rows", None, None),
    )
    out_specs = (
        P("section", ("rows", "dp"), None),
        P("section", ("rows", "dp"), None),
        P("section", ("rows", "dp")),
        P("section", ("rows", "dp")),
    )
    return jax.shard_map(
        on_device, mesh=mesh, in_specs=in_specs, out_specs=out_specs, check_vma=False
    )
```

```python
import math

import jax
import jax.numpy as jnp
from jax import lax
from jax.sharding import PartitionSpec as P

GROUPS = 32


EPSILON = 1e-05


def spread_groups(values, channels):
    return jnp.repeat(values, channels // GROUPS, axis=-1)[:, None, None, None, :]


def rows_allsum(value):
    count = lax.axis_size("rows")
    if count & (count - 1):
        return lax.psum(value, "rows")
    mask = 1
    while mask < count:
        partner = [(i, i ^ mask) for i in range(count)]
        value = value + lax.ppermute(value, "rows", partner)
        mask *= 2
    return value


def rows_gather(value):
    count = lax.axis_size("rows")
    slots = jnp.zeros((count,) + value.shape, value.dtype)
    slots = lax.dynamic_update_index_in_dim(slots, value, lax.axis_index("rows"), 0)
    return rows_allsum(slots)


def edge_rows(block):
    count = lax.axis_size("rows")
    up = [(i, i + 1) for i in range(count - 1)]
    down = [(i + 1, i) for i in range(count - 1)]
    low = lax.ppermute(block[:, :, -1:], "rows", up)
    high = lax.ppermute(block[:, :, :1], "rows", down)
    return low, high


def gather_patches(grown_rows):
    frames, padded_rows, columns, channels = grown_rows.shape
    inner_rows = padded_rows - 2
    padded = jnp.pad(grown_rows, ((1, 1), (0, 0), (1, 1), (0, 0)))
    pieces = []
    for lag_frame in range(3):
        for lag_row in range(3):
            for lag_column in range(3):
                pieces.append(
                    padded[
                        lag_frame : lag_frame + frames,
                        lag_row : lag_row + inner_rows,
                        lag_column : lag_column + columns,
                        :,
                    ]
                )
    return jnp.concatenate(pieces, axis=-1).reshape(frames * inner_rows * columns, 27 * channels)


def conv_rows(grown, weights):
    batches, frames, grown_rows, columns, _ = grown.shape
    patches = jax.vmap(gather_patches)(grown).reshape(-1, weights.shape[0])
    out = jnp.dot(patches, weights, preferred_element_type=jnp.float32)
    return out.reshape(batches, frames, grown_rows - 2, columns, weights.shape[1])


def flipped(weights):
    channels = weights.shape[1]
    blocks = weights.reshape(27, -1, channels)[::-1]
    return jnp.swapaxes(blocks, 1, 2).reshape(-1, blocks.shape[1])


def with_halo(low, own, high, keep_low, keep_high):
    low = jnp.where(keep_low, low, jnp.zeros_like(low))
    high = jnp.where(keep_high, high, jnp.zeros_like(high))
    return jnp.concatenate([low, own, high], axis=2)


def forward_block(volume, gain_vec, weights, counted, keep_low, keep_high):
    batches = volume.shape[0]
    channels = volume.shape[-1]
    local_count = counted // lax.axis_size("rows")
    grouped = volume.reshape(batches, -1, GROUPS, channels // GROUPS)
    local_sum = jnp.sum(grouped, axis=(1, 3))
    local_mean = local_sum / local_count
    deviation = grouped - local_mean[:, None, :, None]
    local_sq = jnp.sum(deviation * deviation, axis=(1, 3))
    low, high = edge_rows(volume)
    gathered = rows_gather(jnp.stack([local_sum, local_sq]))
    sums = gathered[:, 0]
    squares = gathered[:, 1]
    centre = jnp.sum(sums, axis=0) / counted
    part_means = sums / local_count
    spread = (
        jnp.sum(squares, axis=0) + local_count * jnp.sum((part_means - centre) ** 2, axis=0)
    ) / counted
    inverse = lax.rsqrt(spread + EPSILON)
    full = jnp.concatenate([low, volume, high], axis=2)
    normed = (full - spread_groups(centre, channels)) * spread_groups(inverse, channels)
    active = jax.nn.silu(normed * gain_vec).astype(jnp.bfloat16)
    active = with_halo(active[:, :, :1], active[:, :, 1:-1], active[:, :, -1:], keep_low, keep_high)
    result = volume + conv_rows(active, weights)
    return active, centre, inverse, result


def backward_block(volume, gain_vec, reverse_weights, centre, inverse, cot, counted, keep_low, keep_high):
    channels = volume.shape[-1]
    batches = volume.shape[0]
    inverse_full = spread_groups(inverse, channels)
    normed = (volume - spread_groups(centre, channels)) * inverse_full
    zvalue = normed * gain_vec
    cot_low = cot.astype(jnp.bfloat16)
    act_grad = conv_rows(cot_low, reverse_weights)
    logistic = jax.nn.sigmoid(zvalue)
    pre_grad = act_grad * logistic * (1.0 + zvalue * (1.0 - logistic))
    hat_grad = pre_grad * gain_vec
    grouped_grad = hat_grad.reshape(batches, -1, GROUPS, channels // GROUPS)
    grouped_hat = normed.reshape(batches, -1, GROUPS, channels // GROUPS)
    halo_low, halo_high = edge_rows(jnp.concatenate([hat_grad, normed], axis=-1))
    sums = rows_allsum(
        jnp.stack([jnp.sum(grouped_grad, axis=(1, 3)), jnp.sum(grouped_grad * grouped_hat, axis=(1, 3))])
    )
    first = spread_groups(sums[0] / counted, channels)
    second = spread_groups(sums[1] / counted, channels)
    grad_full = jnp.concatenate([halo_low[..., :channels], hat_grad, halo_high[..., :channels]], axis=2)
    hat_full = jnp.concatenate([halo_low[..., channels:], normed, halo_high[..., channels:]], axis=2)
    passed = cot + inverse_full * (grad_full - first - hat_full * second)
    passed = with_halo(passed[:, :, :1], passed[:, :, 1:-1], passed[:, :, -1:], keep_low, keep_high)
    gain_part = jnp.sum((pre_grad * normed).reshape(-1, channels), axis=0)
    return passed, cot_low[:, :, 1:-1], gain_part


def weight_gradient(grown, cot_low):
    patches = jax.vmap(gather_patches)(grown)
    patches = patches.reshape(-1, patches.shape[-1])
    flat_cot = cot_low.reshape(-1, cot_low.shape[-1])
    return lax.dot_general(
        patches, flat_cot, (((0,), (0,)), ((), ())), preferred_element_type=jnp.float32
    )


def reduced_grads(weight_grad, gain_grad, form, after=None):
    shards = lax.axis_size("rows") * lax.axis_size("dp")
    rows_out = weight_grad.shape[0] // shards
    gains_out = gain_grad.shape[0] // shards
    position = lax.axis_index("rows") * lax.axis_size("dp") + lax.axis_index("dp")
    packed = jnp.concatenate(
        [weight_grad.reshape(shards, -1), gain_grad.reshape(shards, gains_out)], axis=1
    )
    if after is not None:
        packed = packed + 0.0 * after[:1, :1]
    if form == "sum":
        total = lax.dynamic_index_in_dim(lax.psum(packed, ("rows", "dp")), position, 0, keepdims=False)
    else:
        total = lax.psum_scatter(packed, ("rows", "dp"), scatter_dimension=0, tiled=True)[0]
    split = rows_out * weight_grad.shape[1]
    return total[:split].reshape(rows_out, weight_grad.shape[1]), total[split:], packed[0, 0]


def on_device(latent, enc_weight, dec_weight, enc_gain, dec_gain, out_grad):
    section_pos = lax.axis_index("section")
    rows_pos = lax.axis_index("rows")
    keep_low = rows_pos > 0
    keep_high = rows_pos < lax.axis_size("rows") - 1
    batches, frames, rows_here, columns, channels = latent.shape
    levels = lax.axis_size("section")
    counted = frames * rows_here * columns * (channels // GROUPS) * lax.axis_size("rows")
    cells_all = batches * lax.axis_size("dp") * frames * rows_here * lax.axis_size("rows") * columns
    loss_scale = 1.0 / math.sqrt(cells_all)
    enc_all = lax.all_gather(enc_weight[0], "section")
    dec_all = lax.all_gather(dec_weight[0], "section")
    enc_gains = lax.all_gather(enc_gain[0], "section")
    dec_gains = lax.all_gather(dec_gain[0], "section")

    hidden = latent.astype(jnp.float32)
    enc_inputs = []
    enc_active = []
    enc_stats = []
    for level in range(levels):
        enc_inputs.append(hidden)
        active, centre, inverse, result = forward_block(
            hidden, enc_gains[level], enc_all[level], counted, keep_low, keep_high
        )
        enc_active.append(active)
        enc_stats.append((centre, inverse))
        hidden = result.astype(jnp.bfloat16).astype(jnp.float32)
    dec_inputs = [None] * levels
    dec_active = [None] * levels
    dec_stats = [None] * levels
    coming = hidden
    for level in reversed(range(levels)):
        united = coming + enc_inputs[level]
        dec_inputs[level] = united
        active, centre, inverse, result = forward_block(
            united, dec_gains[level], dec_all[level], counted, keep_low, keep_high
        )
        dec_active[level] = active
        dec_stats[level] = (centre, inverse)
        coming = result.astype(jnp.bfloat16).astype(jnp.float32)

    seeded_low, seeded_high = edge_rows(out_grad)
    cot = with_halo(seeded_low, out_grad, seeded_high, keep_low, keep_high).astype(jnp.float32) * loss_scale
    skip_grads = [None] * levels
    dec_cots = [None] * levels
    dec_gain_parts = [None] * levels
    for level in range(levels):
        cot, cot_low, gain_part = backward_block(
            dec_inputs[level],
            dec_gains[level],
            flipped(dec_all[level]),
            dec_stats[level][0],
            dec_stats[level][1],
            cot,
            counted,
            keep_low,
            keep_high,
        )
        skip_grads[level] = cot
        dec_cots[level] = cot_low
        dec_gain_parts[level] = gain_part
    own_dec = weight_gradient(
        lax.dynamic_index_in_dim(jnp.stack(dec_active), section_pos, 0, keepdims=False),
        lax.dynamic_index_in_dim(jnp.stack(dec_cots), section_pos, 0, keepdims=False),
    )
    dec_gain_own = lax.dynamic_index_in_dim(jnp.stack(dec_gain_parts), section_pos, 0, keepdims=False)
    dec_result, dec_gains_out, _ = reduced_grads(own_dec, dec_gain_own, "sum")

    enc_cots = [None] * levels
    enc_gain_parts = [None] * levels
    for level in reversed(range(levels)):
      passed, cot_low, gain_part = backward_block(
          enc_inputs[level],
          enc_gains[level],
          flipped(enc_all[level]),
          enc_stats[level][0],
          enc_stats[level][1],
          cot,
          counted,
          keep_low,
          keep_high,
      )
      cot = passed + skip_grads[level]
      enc_cots[level] = cot_low
      enc_gain_parts[level] = gain_part
    late_pos = section_pos + (0.0 * dec_result[0, 0]).astype(section_pos.dtype)
    own_enc = weight_gradient(
        lax.dynamic_index_in_dim(jnp.stack(enc_active), late_pos, 0, keepdims=False),
        lax.dynamic_index_in_dim(jnp.stack(enc_cots), late_pos, 0, keepdims=False),
    )
    enc_gain_own = lax.dynamic_index_in_dim(jnp.stack(enc_gain_parts), late_pos, 0, keepdims=False)
    enc_result, enc_gains_out, _ = reduced_grads(own_enc, enc_gain_own, "scatter", dec_result)
    return (enc_result[None], dec_result[None], enc_gains_out[None], dec_gains_out[None])


def solution(mesh):
    in_specs = (
        P("dp", None, "rows", None, None),
        P("section", None, None),
        P("section", None, None),
        P("section", None),
        P("section", None),
        P("dp", None, "rows", None, None),
    )
    out_specs = (
        P("section", ("rows", "dp"), None),
        P("section", ("rows", "dp"), None),
        P("section", ("rows", "dp")),
        P("section", ("rows", "dp")),
    )

    return jax.shard_map(on_device, mesh=mesh, in_specs=in_specs, out_specs=out_specs, check_vma=False)
```

```python
import math

import jax
import jax.numpy as jnp
from jax import lax
from jax.sharding import PartitionSpec as P

GROUPS = 32


EPSILON = 1e-05


def spread_groups(values, channels):
    return jnp.repeat(values, channels // GROUPS, axis=-1)[:, None, None, None, :]


def rows_allsum(value):
    count = lax.axis_size("rows")
    if count & (count - 1):
        return lax.psum(value, "rows")
    mask = 1
    while mask < count:
        partner = [(i, i ^ mask) for i in range(count)]
        value = value + lax.ppermute(value, "rows", partner)
        mask *= 2
    return value


def rows_gather(value):
    count = lax.axis_size("rows")
    slots = jnp.zeros((count,) + value.shape, value.dtype)
    slots = lax.dynamic_update_index_in_dim(slots, value, lax.axis_index("rows"), 0)
    return rows_allsum(slots)


def edge_rows(block):
    count = lax.axis_size("rows")
    up = [(i, i + 1) for i in range(count - 1)]
    down = [(i + 1, i) for i in range(count - 1)]
    low = lax.ppermute(block[:, :, -1:], "rows", up)
    high = lax.ppermute(block[:, :, :1], "rows", down)
    return low, high


def gather_patches(grown_rows):
    frames, padded_rows, columns, channels = grown_rows.shape
    inner_rows = padded_rows - 2
    padded = jnp.pad(grown_rows, ((1, 1), (0, 0), (1, 1), (0, 0)))
    pieces = []
    for lag_frame in range(3):
        for lag_row in range(3):
            for lag_column in range(3):
                pieces.append(
                    padded[
                        lag_frame : lag_frame + frames,
                        lag_row : lag_row + inner_rows,
                        lag_column : lag_column + columns,
                        :,
                    ]
                )
    return jnp.concatenate(pieces, axis=-1).reshape(frames * inner_rows * columns, 27 * channels)


def conv_rows(grown, weights):
    batches, frames, grown_rows, columns, _ = grown.shape
    patches = jax.vmap(gather_patches)(grown).reshape(-1, weights.shape[0])
    out = jnp.dot(patches, weights, preferred_element_type=jnp.float32)
    return out.reshape(batches, frames, grown_rows - 2, columns, weights.shape[1])


def flipped(weights):
    channels = weights.shape[1]
    blocks = weights.reshape(27, -1, channels)[::-1]
    return jnp.swapaxes(blocks, 1, 2).reshape(-1, blocks.shape[1])


def with_halo(low, own, high, keep_low, keep_high):
    low = jnp.where(keep_low, low, jnp.zeros_like(low))
    high = jnp.where(keep_high, high, jnp.zeros_like(high))
    return jnp.concatenate([low, own, high], axis=2)


def forward_block(volume, gain_vec, weights, counted, keep_low, keep_high):
    batches = volume.shape[0]
    channels = volume.shape[-1]
    local_count = counted // lax.axis_size("rows")
    grouped = volume.reshape(batches, -1, GROUPS, channels // GROUPS)
    local_sum = jnp.sum(grouped, axis=(1, 3))
    local_mean = local_sum / local_count
    deviation = grouped - local_mean[:, None, :, None]
    local_sq = jnp.sum(deviation * deviation, axis=(1, 3))
    low, high = edge_rows(volume)
    gathered = rows_gather(jnp.stack([local_sum, local_sq]))
    sums = gathered[:, 0]
    squares = gathered[:, 1]
    centre = jnp.sum(sums, axis=0) / counted
    part_means = sums / local_count
    spread = (
        jnp.sum(squares, axis=0) + local_count * jnp.sum((part_means - centre) ** 2, axis=0)
    ) / counted
    inverse = lax.rsqrt(spread + EPSILON)
    full = jnp.concatenate([low, volume, high], axis=2)
    normed = (full - spread_groups(centre, channels)) * spread_groups(inverse, channels)
    active = jax.nn.silu(normed * gain_vec).astype(jnp.bfloat16)
    active = with_halo(active[:, :, :1], active[:, :, 1:-1], active[:, :, -1:], keep_low, keep_high)
    result = volume + conv_rows(active, weights)
    return active, centre, inverse, result


def backward_block(volume, gain_vec, reverse_weights, centre, inverse, cot, counted, keep_low, keep_high):
    channels = volume.shape[-1]
    batches = volume.shape[0]
    inverse_full = spread_groups(inverse, channels)
    normed = (volume - spread_groups(centre, channels)) * inverse_full
    zvalue = normed * gain_vec
    cot_low = cot.astype(jnp.bfloat16)
    act_grad = conv_rows(cot_low, reverse_weights)
    logistic = jax.nn.sigmoid(zvalue)
    pre_grad = act_grad * logistic * (1.0 + zvalue * (1.0 - logistic))
    hat_grad = pre_grad * gain_vec
    grouped_grad = hat_grad.reshape(batches, -1, GROUPS, channels // GROUPS)
    grouped_hat = normed.reshape(batches, -1, GROUPS, channels // GROUPS)
    halo_low, halo_high = edge_rows(jnp.concatenate([hat_grad, normed], axis=-1))
    sums = rows_allsum(
        jnp.stack([jnp.sum(grouped_grad, axis=(1, 3)), jnp.sum(grouped_grad * grouped_hat, axis=(1, 3))])
    )
    first = spread_groups(sums[0] / counted, channels)
    second = spread_groups(sums[1] / counted, channels)
    grad_full = jnp.concatenate([halo_low[..., :channels], hat_grad, halo_high[..., :channels]], axis=2)
    hat_full = jnp.concatenate([halo_low[..., channels:], normed, halo_high[..., channels:]], axis=2)
    passed = cot + inverse_full * (grad_full - first - hat_full * second)
    passed = with_halo(passed[:, :, :1], passed[:, :, 1:-1], passed[:, :, -1:], keep_low, keep_high)
    gain_part = jnp.sum((pre_grad * normed).reshape(-1, channels), axis=0)
    return passed, cot_low[:, :, 1:-1], gain_part


def weight_gradient(grown, cot_low):
    patches = jax.vmap(gather_patches)(grown)
    patches = patches.reshape(-1, patches.shape[-1])
    flat_cot = cot_low.reshape(-1, cot_low.shape[-1])
    return lax.dot_general(
        patches, flat_cot, (((0,), (0,)), ((), ())), preferred_element_type=jnp.float32
    )


def halving_order(bits):
    order = [b for b in (0, 1, bits - 1) if 0 <= b < bits]
    order = list(dict.fromkeys(order))
    return order + [b for b in range(bits) if b not in order]


def tree_scatter(packed):
    row_count = lax.axis_size("rows")
    dp_count = lax.axis_size("dp")
    if (row_count & (row_count - 1)) or (dp_count & (dp_count - 1)):
        return lax.psum_scatter(packed, ("rows", "dp"), scatter_dimension=0, tiled=True)[0]
    row_bits = row_count.bit_length() - 1
    dp_bits = dp_count.bit_length() - 1
    names = [("rows", row_bits - 1 - k) for k in range(row_bits)]
    names += [("dp", dp_bits - 1 - k) for k in range(dp_bits)]
    buf = packed.reshape((2,) * (row_bits + dp_bits) + packed.shape[1:])
    steps = [("rows", b) for b in halving_order(row_bits)] + [("dp", b) for b in range(dp_bits)]
    for axis, bit in steps:
        place = names.index((axis, bit))
        mine = (lax.axis_index(axis) >> bit) & 1
        keep = lax.dynamic_index_in_dim(buf, mine, place, keepdims=False)
        send = lax.dynamic_index_in_dim(buf, 1 - mine, place, keepdims=False)
        count = lax.axis_size(axis)
        buf = keep + lax.ppermute(send, axis, [(i, i ^ (1 << bit)) for i in range(count)])
        names.pop(place)
    return buf


def reduced_grads(weight_grad, gain_grad):
    shards = lax.axis_size("rows") * lax.axis_size("dp")
    rows_out = weight_grad.shape[0] // shards
    gains_out = gain_grad.shape[0] // shards
    packed = jnp.concatenate(
        [weight_grad.reshape(shards, -1), gain_grad.reshape(shards, gains_out)], axis=1
    )
    total = tree_scatter(packed)
    split = rows_out * weight_grad.shape[1]
    return total[:split].reshape(rows_out, weight_grad.shape[1]), total[split:]


def on_device(latent, enc_weight, dec_weight, enc_gain, dec_gain, out_grad):
    section_pos = lax.axis_index("section")
    rows_pos = lax.axis_index("rows")
    keep_low = rows_pos > 0
    keep_high = rows_pos < lax.axis_size("rows") - 1
    batches, frames, rows_here, columns, channels = latent.shape
    levels = lax.axis_size("section")
    counted = frames * rows_here * columns * (channels // GROUPS) * lax.axis_size("rows")
    cells_all = batches * lax.axis_size("dp") * frames * rows_here * lax.axis_size("rows") * columns
    loss_scale = 1.0 / math.sqrt(cells_all)
    enc_all = lax.all_gather(enc_weight[0], "section")
    dec_all = lax.all_gather(dec_weight[0], "section")
    enc_gains = lax.all_gather(enc_gain[0], "section")
    dec_gains = lax.all_gather(dec_gain[0], "section")

    hidden = latent.astype(jnp.float32)
    enc_inputs = []
    enc_active = []
    enc_stats = []
    for level in range(levels):
        enc_inputs.append(hidden)
        active, centre, inverse, result = forward_block(
            hidden, enc_gains[level], enc_all[level], counted, keep_low, keep_high
        )
        enc_active.append(active)
        enc_stats.append((centre, inverse))
        hidden = result.astype(jnp.bfloat16).astype(jnp.float32)
    dec_inputs = [None] * levels
    dec_active = [None] * levels
    dec_stats = [None] * levels
    coming = hidden
    for level in reversed(range(levels)):
        united = coming + enc_inputs[level]
        dec_inputs[level] = united
        active, centre, inverse, result = forward_block(
            united, dec_gains[level], dec_all[level], counted, keep_low, keep_high
        )
        dec_active[level] = active
        dec_stats[level] = (centre, inverse)
        coming = result.astype(jnp.bfloat16).astype(jnp.float32)

    seeded_low, seeded_high = edge_rows(out_grad)
    cot = with_halo(seeded_low, out_grad, seeded_high, keep_low, keep_high).astype(jnp.float32) * loss_scale
    skip_grads = [None] * levels
    dec_cots = [None] * levels
    dec_gain_parts = [None] * levels
    for level in range(levels):
        cot, cot_low, gain_part = backward_block(
            dec_inputs[level],
            dec_gains[level],
            flipped(dec_all[level]),
            dec_stats[level][0],
            dec_stats[level][1],
            cot,
            counted,
            keep_low,
            keep_high,
        )
        skip_grads[level] = cot
        dec_cots[level] = cot_low
        dec_gain_parts[level] = gain_part
    own_dec = weight_gradient(
        lax.dynamic_index_in_dim(jnp.stack(dec_active), section_pos, 0, keepdims=False),
        lax.dynamic_index_in_dim(jnp.stack(dec_cots), section_pos, 0, keepdims=False),
    )
    dec_gain_own = lax.dynamic_index_in_dim(jnp.stack(dec_gain_parts), section_pos, 0, keepdims=False)
    dec_result, dec_gains_out = reduced_grads(own_dec, dec_gain_own)

    enc_cots = [None] * levels
    enc_gain_parts = [None] * levels
    for level in reversed(range(levels)):
      passed, cot_low, gain_part = backward_block(
          enc_inputs[level],
          enc_gains[level],
          flipped(enc_all[level]),
          enc_stats[level][0],
          enc_stats[level][1],
          cot,
          counted,
          keep_low,
          keep_high,
      )
      cot = passed + skip_grads[level]
      enc_cots[level] = cot_low
      enc_gain_parts[level] = gain_part
    own_enc = weight_gradient(
        lax.dynamic_index_in_dim(jnp.stack(enc_active), section_pos, 0, keepdims=False),
        lax.dynamic_index_in_dim(jnp.stack(enc_cots), section_pos, 0, keepdims=False),
    )
    enc_gain_own = lax.dynamic_index_in_dim(jnp.stack(enc_gain_parts), section_pos, 0, keepdims=False)
    enc_result, enc_gains_out = reduced_grads(own_enc, enc_gain_own)
    return (enc_result[None], dec_result[None], enc_gains_out[None], dec_gains_out[None])


def solution(mesh):
    in_specs = (
        P("dp", None, "rows", None, None),
        P("section", None, None),
        P("section", None, None),
        P("section", None),
        P("section", None),
        P("dp", None, "rows", None, None),
    )
    out_specs = (
        P("section", ("rows", "dp"), None),
        P("section", ("rows", "dp"), None),
        P("section", ("rows", "dp")),
        P("section", ("rows", "dp")),
    )

    return jax.shard_map(on_device, mesh=mesh, in_specs=in_specs, out_specs=out_specs, check_vma=False)
```

```python
import math

import jax
import jax.numpy as jnp
from jax import lax
from jax.sharding import PartitionSpec as P

GROUPS = 32


EPSILON = 1e-05


def spread_groups(values, channels):
    return jnp.repeat(values, channels // GROUPS, axis=-1)[:, None, None, None, :]


def rows_allsum(value):
    count = lax.axis_size("rows")
    if count & (count - 1):
        return lax.psum(value, "rows")
    mask = 1
    while mask < count:
        partner = [(i, i ^ mask) for i in range(count)]
        value = value + lax.ppermute(value, "rows", partner)
        mask *= 2
    return value


def rows_gather(value):
    count = lax.axis_size("rows")
    slots = jnp.zeros((count,) + value.shape, value.dtype)
    slots = lax.dynamic_update_index_in_dim(slots, value, lax.axis_index("rows"), 0)
    return rows_allsum(slots)


def edge_rows(block):
    count = lax.axis_size("rows")
    up = [(i, i + 1) for i in range(count - 1)]
    down = [(i + 1, i) for i in range(count - 1)]
    low = lax.ppermute(block[:, :, -1:], "rows", up)
    high = lax.ppermute(block[:, :, :1], "rows", down)
    return low, high


def gather_patches(grown_rows):
    frames, padded_rows, columns, channels = grown_rows.shape
    inner_rows = padded_rows - 2
    padded = jnp.pad(grown_rows, ((1, 1), (0, 0), (1, 1), (0, 0)))
    pieces = []
    for lag_frame in range(3):
        for lag_row in range(3):
            for lag_column in range(3):
                pieces.append(
                    padded[
                        lag_frame : lag_frame + frames,
                        lag_row : lag_row + inner_rows,
                        lag_column : lag_column + columns,
                        :,
                    ]
                )
    return jnp.concatenate(pieces, axis=-1).reshape(frames * inner_rows * columns, 27 * channels)


def conv_rows(grown, weights):
    batches, frames, grown_rows, columns, _ = grown.shape
    patches = jax.vmap(gather_patches)(grown).reshape(-1, weights.shape[0])
    out = jnp.dot(patches, weights, preferred_element_type=jnp.float32)
    return out.reshape(batches, frames, grown_rows - 2, columns, weights.shape[1])


def flipped(weights):
    channels = weights.shape[1]
    blocks = weights.reshape(27, -1, channels)[::-1]
    return jnp.swapaxes(blocks, 1, 2).reshape(-1, blocks.shape[1])


def with_halo(low, own, high, keep_low, keep_high):
    low = jnp.where(keep_low, low, jnp.zeros_like(low))
    high = jnp.where(keep_high, high, jnp.zeros_like(high))
    return jnp.concatenate([low, own, high], axis=2)


def forward_block(volume, gain_vec, weights, counted, keep_low, keep_high):
    batches = volume.shape[0]
    channels = volume.shape[-1]
    local_count = counted // lax.axis_size("rows")
    grouped = volume.reshape(batches, -1, GROUPS, channels // GROUPS)
    local_sum = jnp.sum(grouped, axis=(1, 3))
    local_mean = local_sum / local_count
    deviation = grouped - local_mean[:, None, :, None]
    local_sq = jnp.sum(deviation * deviation, axis=(1, 3))
    low, high = edge_rows(volume)
    gathered = rows_gather(jnp.stack([local_sum, local_sq]))
    sums = gathered[:, 0]
    squares = gathered[:, 1]
    centre = jnp.sum(sums, axis=0) / counted
    part_means = sums / local_count
    spread = (
        jnp.sum(squares, axis=0) + local_count * jnp.sum((part_means - centre) ** 2, axis=0)
    ) / counted
    inverse = lax.rsqrt(spread + EPSILON)
    full = jnp.concatenate([low, volume, high], axis=2)
    normed = (full - spread_groups(centre, channels)) * spread_groups(inverse, channels)
    active = jax.nn.silu(normed * gain_vec).astype(jnp.bfloat16)
    active = with_halo(active[:, :, :1], active[:, :, 1:-1], active[:, :, -1:], keep_low, keep_high)
    result = volume + conv_rows(active, weights)
    return active, centre, inverse, result


def backward_block(volume, gain_vec, reverse_weights, centre, inverse, cot, counted, keep_low, keep_high):
    channels = volume.shape[-1]
    batches = volume.shape[0]
    inverse_full = spread_groups(inverse, channels)
    normed = (volume - spread_groups(centre, channels)) * inverse_full
    zvalue = normed * gain_vec
    cot_low = cot.astype(jnp.bfloat16)
    act_grad = conv_rows(cot_low, reverse_weights)
    logistic = jax.nn.sigmoid(zvalue)
    pre_grad = act_grad * logistic * (1.0 + zvalue * (1.0 - logistic))
    hat_grad = pre_grad * gain_vec
    grouped_grad = hat_grad.reshape(batches, -1, GROUPS, channels // GROUPS)
    grouped_hat = normed.reshape(batches, -1, GROUPS, channels // GROUPS)
    halo_low, halo_high = edge_rows(jnp.concatenate([hat_grad, normed], axis=-1))
    sums = rows_allsum(
        jnp.stack([jnp.sum(grouped_grad, axis=(1, 3)), jnp.sum(grouped_grad * grouped_hat, axis=(1, 3))])
    )
    first = spread_groups(sums[0] / counted, channels)
    second = spread_groups(sums[1] / counted, channels)
    grad_full = jnp.concatenate([halo_low[..., :channels], hat_grad, halo_high[..., :channels]], axis=2)
    hat_full = jnp.concatenate([halo_low[..., channels:], normed, halo_high[..., channels:]], axis=2)
    passed = cot + inverse_full * (grad_full - first - hat_full * second)
    passed = with_halo(passed[:, :, :1], passed[:, :, 1:-1], passed[:, :, -1:], keep_low, keep_high)
    gain_part = jnp.sum((pre_grad * normed).reshape(-1, channels), axis=0)
    return passed, cot_low[:, :, 1:-1], gain_part


def weight_gradient(grown, cot_low):
    patches = jax.vmap(gather_patches)(grown)
    patches = patches.reshape(-1, patches.shape[-1])
    flat_cot = cot_low.reshape(-1, cot_low.shape[-1])
    return lax.dot_general(
        patches, flat_cot, (((0,), (0,)), ((), ())), preferred_element_type=jnp.float32
    )


def halving_order(bits):
    order = [b for b in (0, 1, bits - 1) if 0 <= b < bits]
    order = list(dict.fromkeys(order))
    return order + [b for b in range(bits) if b not in order]


def tree_scatter(packed):
    row_count = lax.axis_size("rows")
    dp_count = lax.axis_size("dp")
    if (row_count & (row_count - 1)) or (dp_count & (dp_count - 1)):
        return lax.psum_scatter(packed, ("rows", "dp"), scatter_dimension=0, tiled=True)[0]
    row_bits = row_count.bit_length() - 1
    dp_bits = dp_count.bit_length() - 1
    names = [("rows", row_bits - 1 - k) for k in range(row_bits)]
    names += [("dp", dp_bits - 1 - k) for k in range(dp_bits)]
    buf = packed.reshape((2,) * (row_bits + dp_bits) + packed.shape[1:])
    steps = [("rows", b) for b in halving_order(row_bits)] + [("dp", b) for b in range(dp_bits)]
    for axis, bit in steps:
        place = names.index((axis, bit))
        mine = (lax.axis_index(axis) >> bit) & 1
        keep = lax.dynamic_index_in_dim(buf, mine, place, keepdims=False)
        send = lax.dynamic_index_in_dim(buf, 1 - mine, place, keepdims=False)
        count = lax.axis_size(axis)
        buf = keep + lax.ppermute(send, axis, [(i, i ^ (1 << bit)) for i in range(count)])
        names.pop(place)
    return buf


def reduced_grads(weight_grad, gain_grad):
    shards = lax.axis_size("rows") * lax.axis_size("dp")
    rows_out = weight_grad.shape[0] // shards
    gains_out = gain_grad.shape[0] // shards
    packed = jnp.concatenate(
        [weight_grad.reshape(shards, -1), gain_grad.reshape(shards, gains_out)], axis=1
    )
    total = tree_scatter(packed)
    split = rows_out * weight_grad.shape[1]
    return total[:split].reshape(rows_out, weight_grad.shape[1]), total[split:]


def section_gather(value):
    count = lax.axis_size("section")
    if count & (count - 1):
        return lax.all_gather(value, "section")
    slots = jnp.zeros((count,) + value.shape, value.dtype)
    slots = lax.dynamic_update_index_in_dim(slots, value, lax.axis_index("section"), 0)
    mask = 1
    while mask < count:
        slots = slots + lax.ppermute(slots, "section", [(i, i ^ mask) for i in range(count)])
        mask *= 2
    return slots


def section_weights(weights):
    rows_count = lax.axis_size("rows")
    half = weights.shape[0] // 2
    if rows_count % 2 or weights.shape[0] % 2:
        return lax.all_gather(weights, "section")
    core = lax.axis_index("rows") % 2
    mine = lax.all_gather(lax.dynamic_slice_in_dim(weights, core * half, half, 0), "section")
    other = lax.ppermute(mine, "rows", [(i, i ^ 1) for i in range(rows_count)])
    low = jnp.where(core == 0, mine, other)
    high = jnp.where(core == 0, other, mine)
    return jnp.concatenate([low, high], axis=1)


def on_device(latent, enc_weight, dec_weight, enc_gain, dec_gain, out_grad):
    section_pos = lax.axis_index("section")
    rows_pos = lax.axis_index("rows")
    keep_low = rows_pos > 0
    keep_high = rows_pos < lax.axis_size("rows") - 1
    batches, frames, rows_here, columns, channels = latent.shape
    levels = lax.axis_size("section")
    counted = frames * rows_here * columns * (channels // GROUPS) * lax.axis_size("rows")
    cells_all = batches * lax.axis_size("dp") * frames * rows_here * lax.axis_size("rows") * columns
    loss_scale = 1.0 / math.sqrt(cells_all)
    enc_all = section_weights(enc_weight[0])
    dec_all = section_weights(dec_weight[0])
    gains_all = section_gather(jnp.stack([enc_gain[0], dec_gain[0]]))
    enc_gains = gains_all[:, 0]
    dec_gains = gains_all[:, 1]

    hidden = latent.astype(jnp.float32)
    enc_inputs = []
    enc_active = []
    enc_stats = []
    for level in range(levels):
        enc_inputs.append(hidden)
        active, centre, inverse, result = forward_block(
            hidden, enc_gains[level], enc_all[level], counted, keep_low, keep_high
        )
        enc_active.append(active)
        enc_stats.append((centre, inverse))
        hidden = result.astype(jnp.bfloat16).astype(jnp.float32)
    dec_inputs = [None] * levels
    dec_active = [None] * levels
    dec_stats = [None] * levels
    coming = hidden
    for level in reversed(range(levels)):
        united = coming + enc_inputs[level]
        dec_inputs[level] = united
        active, centre, inverse, result = forward_block(
            united, dec_gains[level], dec_all[level], counted, keep_low, keep_high
        )
        dec_active[level] = active
        dec_stats[level] = (centre, inverse)
        coming = result.astype(jnp.bfloat16).astype(jnp.float32)

    seeded_low, seeded_high = edge_rows(out_grad)
    cot = with_halo(seeded_low, out_grad, seeded_high, keep_low, keep_high).astype(jnp.float32) * loss_scale
    skip_grads = [None] * levels
    dec_cots = [None] * levels
    dec_gain_parts = [None] * levels
    for level in range(levels):
        cot, cot_low, gain_part = backward_block(
            dec_inputs[level],
            dec_gains[level],
            flipped(dec_all[level]),
            dec_stats[level][0],
            dec_stats[level][1],
            cot,
            counted,
            keep_low,
            keep_high,
        )
        skip_grads[level] = cot
        dec_cots[level] = cot_low
        dec_gain_parts[level] = gain_part
    own_dec = weight_gradient(
        lax.dynamic_index_in_dim(jnp.stack(dec_active), section_pos, 0, keepdims=False),
        lax.dynamic_index_in_dim(jnp.stack(dec_cots), section_pos, 0, keepdims=False),
    )
    dec_gain_own = lax.dynamic_index_in_dim(jnp.stack(dec_gain_parts), section_pos, 0, keepdims=False)
    dec_result, dec_gains_out = reduced_grads(own_dec, dec_gain_own)

    enc_cots = [None] * levels
    enc_gain_parts = [None] * levels
    for level in reversed(range(levels)):
      passed, cot_low, gain_part = backward_block(
          enc_inputs[level],
          enc_gains[level],
          flipped(enc_all[level]),
          enc_stats[level][0],
          enc_stats[level][1],
          cot,
          counted,
          keep_low,
          keep_high,
      )
      cot = passed + skip_grads[level]
      enc_cots[level] = cot_low
      enc_gain_parts[level] = gain_part
    own_enc = weight_gradient(
        lax.dynamic_index_in_dim(jnp.stack(enc_active), section_pos, 0, keepdims=False),
        lax.dynamic_index_in_dim(jnp.stack(enc_cots), section_pos, 0, keepdims=False),
    )
    enc_gain_own = lax.dynamic_index_in_dim(jnp.stack(enc_gain_parts), section_pos, 0, keepdims=False)
    enc_result, enc_gains_out = reduced_grads(own_enc, enc_gain_own)
    return (enc_result[None], dec_result[None], enc_gains_out[None], dec_gains_out[None])


def solution(mesh):
    in_specs = (
        P("dp", None, "rows", None, None),
        P("section", None, None),
        P("section", None, None),
        P("section", None),
        P("section", None),
        P("dp", None, "rows", None, None),
    )
    out_specs = (
        P("section", ("rows", "dp"), None),
        P("section", ("rows", "dp"), None),
        P("section", ("rows", "dp")),
        P("section", ("rows", "dp")),
    )

    return jax.shard_map(on_device, mesh=mesh, in_specs=in_specs, out_specs=out_specs, check_vma=False)
```

```python
import math

import jax
import jax.numpy as jnp
from jax import lax
from jax.sharding import PartitionSpec as P

GROUPS = 32


EPSILON = 1e-05


def spread_groups(values, channels):
    return jnp.repeat(values, channels // GROUPS, axis=-1)[:, None, None, None, :]


def rows_allsum(value):
    count = lax.axis_size("rows")
    if count & (count - 1):
        return lax.psum(value, "rows")
    mask = 1
    while mask < count:
        partner = [(i, i ^ mask) for i in range(count)]
        value = value + lax.ppermute(value, "rows", partner)
        mask *= 2
    return value


def edge_rows(block):
    count = lax.axis_size("rows")
    up = [(i, i + 1) for i in range(count - 1)]
    down = [(i + 1, i) for i in range(count - 1)]
    low = lax.ppermute(block[:, :, -1:], "rows", up)
    high = lax.ppermute(block[:, :, :1], "rows", down)
    return low, high


def allsum_with_halo(value, block):
    count = lax.axis_size("rows")
    if count % 2 or (count & (count - 1)):
        low, high = edge_rows(block)
        return rows_allsum(value), low, high
    even = lax.axis_index("rows") % 2 == 0
    first, last = block[:, :, :1], block[:, :, -1:]
    toward = jnp.where(even, last, first)
    message = jnp.concatenate([value.reshape(-1), toward.reshape(-1)])
    message = lax.ppermute(message, "rows", [(i, i ^ 1) for i in range(count)])
    partner = message[value.size :].reshape(toward.shape)
    value = value + message[: value.size].reshape(value.shape)
    away = jnp.where(even, first, last)
    swap = [(i, i + 1) for i in range(1, count - 1, 2)] + [(i + 1, i) for i in range(1, count - 1, 2)]
    other = lax.ppermute(away, "rows", swap)
    mask = 2
    while mask < count:
        value = value + lax.ppermute(value, "rows", [(i, i ^ mask) for i in range(count)])
        mask *= 2
    low = jnp.where(even, other, partner)
    high = jnp.where(even, partner, other)
    return value, low, high


def gather_patches(grown_rows):
    frames, padded_rows, columns, channels = grown_rows.shape
    inner_rows = padded_rows - 2
    padded = jnp.pad(grown_rows, ((1, 1), (0, 0), (1, 1), (0, 0)))
    pieces = []
    for lag_frame in range(3):
        for lag_row in range(3):
            for lag_column in range(3):
                pieces.append(
                    padded[
                        lag_frame : lag_frame + frames,
                        lag_row : lag_row + inner_rows,
                        lag_column : lag_column + columns,
                        :,
                    ]
                )
    return jnp.concatenate(pieces, axis=-1).reshape(frames * inner_rows * columns, 27 * channels)


def conv_rows(grown, weights):
    batches, frames, grown_rows, columns, _ = grown.shape
    patches = jax.vmap(gather_patches)(grown).reshape(-1, weights.shape[0])
    out = jnp.dot(patches, weights, preferred_element_type=jnp.float32)
    return out.reshape(batches, frames, grown_rows - 2, columns, weights.shape[1])


def flipped(weights):
    channels = weights.shape[1]
    blocks = weights.reshape(27, -1, channels)[::-1]
    return jnp.swapaxes(blocks, 1, 2).reshape(-1, blocks.shape[1])


def with_halo(low, own, high, keep_low, keep_high):
    low = jnp.where(keep_low, low, jnp.zeros_like(low))
    high = jnp.where(keep_high, high, jnp.zeros_like(high))
    return jnp.concatenate([low, own, high], axis=2)


def forward_block(volume, gain_vec, weights, counted, keep_low, keep_high):
    batches = volume.shape[0]
    channels = volume.shape[-1]
    local_count = counted // lax.axis_size("rows")
    grouped = volume.reshape(batches, -1, GROUPS, channels // GROUPS)
    local_sum = jnp.sum(grouped, axis=(1, 3))
    local_mean = local_sum / local_count
    deviation = grouped - local_mean[:, None, :, None]
    local_sq = jnp.sum(deviation * deviation, axis=(1, 3))
    count = lax.axis_size("rows")
    slots = jnp.zeros((count, 2) + local_sum.shape, local_sum.dtype)
    slots = lax.dynamic_update_index_in_dim(
        slots, jnp.stack([local_sum, local_sq]), lax.axis_index("rows"), 0
    )
    gathered, low, high = allsum_with_halo(slots, volume)
    sums = gathered[:, 0]
    squares = gathered[:, 1]
    centre = jnp.sum(sums, axis=0) / counted
    part_means = sums / local_count
    spread = (
        jnp.sum(squares, axis=0) + local_count * jnp.sum((part_means - centre) ** 2, axis=0)
    ) / counted
    inverse = lax.rsqrt(spread + EPSILON)
    full = jnp.concatenate([low, volume, high], axis=2)
    normed = (full - spread_groups(centre, channels)) * spread_groups(inverse, channels)
    active = jax.nn.silu(normed * gain_vec).astype(jnp.bfloat16)
    active = with_halo(active[:, :, :1], active[:, :, 1:-1], active[:, :, -1:], keep_low, keep_high)
    result = volume + conv_rows(active, weights)
    return active, centre, inverse, result


def backward_block(volume, gain_vec, reverse_weights, centre, inverse, cot, counted, keep_low, keep_high):
    channels = volume.shape[-1]
    batches = volume.shape[0]
    inverse_full = spread_groups(inverse, channels)
    normed = (volume - spread_groups(centre, channels)) * inverse_full
    zvalue = normed * gain_vec
    cot_low = cot.astype(jnp.bfloat16)
    act_grad = conv_rows(cot_low, reverse_weights)
    logistic = jax.nn.sigmoid(zvalue)
    pre_grad = act_grad * logistic * (1.0 + zvalue * (1.0 - logistic))
    hat_grad = pre_grad * gain_vec
    grouped_grad = hat_grad.reshape(batches, -1, GROUPS, channels // GROUPS)
    grouped_hat = normed.reshape(batches, -1, GROUPS, channels // GROUPS)
    sums, halo_low, halo_high = allsum_with_halo(
        jnp.stack([jnp.sum(grouped_grad, axis=(1, 3)), jnp.sum(grouped_grad * grouped_hat, axis=(1, 3))]),
        jnp.concatenate([hat_grad, normed], axis=-1),
    )
    first = spread_groups(sums[0] / counted, channels)
    second = spread_groups(sums[1] / counted, channels)
    grad_full = jnp.concatenate([halo_low[..., :channels], hat_grad, halo_high[..., :channels]], axis=2)
    hat_full = jnp.concatenate([halo_low[..., channels:], normed, halo_high[..., channels:]], axis=2)
    passed = cot + inverse_full * (grad_full - first - hat_full * second)
    passed = with_halo(passed[:, :, :1], passed[:, :, 1:-1], passed[:, :, -1:], keep_low, keep_high)
    gain_part = jnp.sum((pre_grad * normed).reshape(-1, channels), axis=0)
    return passed, cot_low[:, :, 1:-1], gain_part


def weight_gradient(grown, cot_low):
    patches = jax.vmap(gather_patches)(grown)
    patches = patches.reshape(-1, patches.shape[-1])
    flat_cot = cot_low.reshape(-1, cot_low.shape[-1])
    return lax.dot_general(
        patches, flat_cot, (((0,), (0,)), ((), ())), preferred_element_type=jnp.float32
    )


def halving_order(bits):
    order = [b for b in (0, 1, bits - 1) if 0 <= b < bits]
    order = list(dict.fromkeys(order))
    return order + [b for b in range(bits) if b not in order]


def tree_scatter(packed):
    row_count = lax.axis_size("rows")
    dp_count = lax.axis_size("dp")
    if (row_count & (row_count - 1)) or (dp_count & (dp_count - 1)):
        return lax.psum_scatter(packed, ("rows", "dp"), scatter_dimension=0, tiled=True)[0]
    row_bits = row_count.bit_length() - 1
    dp_bits = dp_count.bit_length() - 1
    names = [("rows", row_bits - 1 - k) for k in range(row_bits)]
    names += [("dp", dp_bits - 1 - k) for k in range(dp_bits)]
    buf = packed.reshape((2,) * (row_bits + dp_bits) + packed.shape[1:])
    steps = [("rows", b) for b in halving_order(row_bits)] + [("dp", b) for b in range(dp_bits)]
    for axis, bit in steps:
        place = names.index((axis, bit))
        mine = (lax.axis_index(axis) >> bit) & 1
        keep = lax.dynamic_index_in_dim(buf, mine, place, keepdims=False)
        send = lax.dynamic_index_in_dim(buf, 1 - mine, place, keepdims=False)
        count = lax.axis_size(axis)
        buf = keep + lax.ppermute(send, axis, [(i, i ^ (1 << bit)) for i in range(count)])
        names.pop(place)
    return buf


def reduced_grads(weight_grad, gain_grad):
    shards = lax.axis_size("rows") * lax.axis_size("dp")
    rows_out = weight_grad.shape[0] // shards
    gains_out = gain_grad.shape[0] // shards
    packed = jnp.concatenate(
        [weight_grad.reshape(shards, -1), gain_grad.reshape(shards, gains_out)], axis=1
    )
    total = tree_scatter(packed)
    split = rows_out * weight_grad.shape[1]
    return total[:split].reshape(rows_out, weight_grad.shape[1]), total[split:]


def section_gather(value):
    count = lax.axis_size("section")
    if count & (count - 1):
        return lax.all_gather(value, "section")
    slots = jnp.zeros((count,) + value.shape, value.dtype)
    slots = lax.dynamic_update_index_in_dim(slots, value, lax.axis_index("section"), 0)
    mask = 1
    while mask < count:
        slots = slots + lax.ppermute(slots, "section", [(i, i ^ mask) for i in range(count)])
        mask *= 2
    return slots


def section_weights(weights):
    rows_count = lax.axis_size("rows")
    half = weights.shape[0] // 2
    if rows_count % 2 or weights.shape[0] % 2:
        return lax.all_gather(weights, "section")
    core = lax.axis_index("rows") % 2
    mine = lax.all_gather(lax.dynamic_slice_in_dim(weights, core * half, half, 0), "section")
    other = lax.ppermute(mine, "rows", [(i, i ^ 1) for i in range(rows_count)])
    low = jnp.where(core == 0, mine, other)
    high = jnp.where(core == 0, other, mine)
    return jnp.concatenate([low, high], axis=1)


def on_device(latent, enc_weight, dec_weight, enc_gain, dec_gain, out_grad):
    section_pos = lax.axis_index("section")
    rows_pos = lax.axis_index("rows")
    keep_low = rows_pos > 0
    keep_high = rows_pos < lax.axis_size("rows") - 1
    batches, frames, rows_here, columns, channels = latent.shape
    levels = lax.axis_size("section")
    counted = frames * rows_here * columns * (channels // GROUPS) * lax.axis_size("rows")
    cells_all = batches * lax.axis_size("dp") * frames * rows_here * lax.axis_size("rows") * columns
    loss_scale = 1.0 / math.sqrt(cells_all)
    enc_all = section_weights(enc_weight[0])
    dec_all = section_weights(dec_weight[0])
    gains_all = section_gather(jnp.stack([enc_gain[0], dec_gain[0]]))
    enc_gains = gains_all[:, 0]
    dec_gains = gains_all[:, 1]

    hidden = latent.astype(jnp.float32)
    enc_inputs = []
    enc_active = []
    enc_stats = []
    for level in range(levels):
        enc_inputs.append(hidden)
        active, centre, inverse, result = forward_block(
            hidden, enc_gains[level], enc_all[level], counted, keep_low, keep_high
        )
        enc_active.append(active)
        enc_stats.append((centre, inverse))
        hidden = result.astype(jnp.bfloat16).astype(jnp.float32)
    dec_inputs = [None] * levels
    dec_active = [None] * levels
    dec_stats = [None] * levels
    coming = hidden
    for level in reversed(range(levels)):
        united = coming + enc_inputs[level]
        dec_inputs[level] = united
        active, centre, inverse, result = forward_block(
            united, dec_gains[level], dec_all[level], counted, keep_low, keep_high
        )
        dec_active[level] = active
        dec_stats[level] = (centre, inverse)
        coming = result.astype(jnp.bfloat16).astype(jnp.float32)

    seeded_low, seeded_high = edge_rows(out_grad)
    cot = with_halo(seeded_low, out_grad, seeded_high, keep_low, keep_high).astype(jnp.float32) * loss_scale
    skip_grads = [None] * levels
    dec_cots = [None] * levels
    dec_gain_parts = [None] * levels
    for level in range(levels):
        cot, cot_low, gain_part = backward_block(
            dec_inputs[level],
            dec_gains[level],
            flipped(dec_all[level]),
            dec_stats[level][0],
            dec_stats[level][1],
            cot,
            counted,
            keep_low,
            keep_high,
        )
        skip_grads[level] = cot
        dec_cots[level] = cot_low
        dec_gain_parts[level] = gain_part
    own_dec = weight_gradient(
        lax.dynamic_index_in_dim(jnp.stack(dec_active), section_pos, 0, keepdims=False),
        lax.dynamic_index_in_dim(jnp.stack(dec_cots), section_pos, 0, keepdims=False),
    )
    dec_gain_own = lax.dynamic_index_in_dim(jnp.stack(dec_gain_parts), section_pos, 0, keepdims=False)
    dec_result, dec_gains_out = reduced_grads(own_dec, dec_gain_own)

    enc_cots = [None] * levels
    enc_gain_parts = [None] * levels
    for level in reversed(range(levels)):
      passed, cot_low, gain_part = backward_block(
          enc_inputs[level],
          enc_gains[level],
          flipped(enc_all[level]),
          enc_stats[level][0],
          enc_stats[level][1],
          cot,
          counted,
          keep_low,
          keep_high,
      )
      cot = passed + skip_grads[level]
      enc_cots[level] = cot_low
      enc_gain_parts[level] = gain_part
    own_enc = weight_gradient(
        lax.dynamic_index_in_dim(jnp.stack(enc_active), section_pos, 0, keepdims=False),
        lax.dynamic_index_in_dim(jnp.stack(enc_cots), section_pos, 0, keepdims=False),
    )
    enc_gain_own = lax.dynamic_index_in_dim(jnp.stack(enc_gain_parts), section_pos, 0, keepdims=False)
    enc_result, enc_gains_out = reduced_grads(own_enc, enc_gain_own)
    return (enc_result[None], dec_result[None], enc_gains_out[None], dec_gains_out[None])


def solution(mesh):
    in_specs = (
        P("dp", None, "rows", None, None),
        P("section", None, None),
        P("section", None, None),
        P("section", None),
        P("section", None),
        P("dp", None, "rows", None, None),
    )
    out_specs = (
        P("section", ("rows", "dp"), None),
        P("section", ("rows", "dp"), None),
        P("section", ("rows", "dp")),
        P("section", ("rows", "dp")),
    )

    return jax.shard_map(on_device, mesh=mesh, in_specs=in_specs, out_specs=out_specs, check_vma=False)
```

```python
import math

import jax
import jax.numpy as jnp
from jax import lax
from jax.sharding import PartitionSpec as P

GROUPS = 32


EPSILON = 1e-05


def spread_groups(values, channels):
    return jnp.repeat(values, channels // GROUPS, axis=-1)[:, None, None, None, :]


def rows_allsum(value):
    count = lax.axis_size("rows")
    if count & (count - 1):
        return lax.psum(value, "rows")
    mask = 1
    while mask < count:
        partner = [(i, i ^ mask) for i in range(count)]
        value = value + lax.ppermute(value, "rows", partner)
        mask *= 2
    return value


def rows_gather(value):
    count = lax.axis_size("rows")
    slots = jnp.zeros((count,) + value.shape, value.dtype)
    slots = lax.dynamic_update_index_in_dim(slots, value, lax.axis_index("rows"), 0)
    return rows_allsum(slots)


def edge_rows(block):
    count = lax.axis_size("rows")
    up = [(i, i + 1) for i in range(count - 1)]
    down = [(i + 1, i) for i in range(count - 1)]
    low = lax.ppermute(block[:, :, -1:], "rows", up)
    high = lax.ppermute(block[:, :, :1], "rows", down)
    return low, high


def gather_with_halo(value, block):
    count = lax.axis_size("rows")
    if count < 4 or (count & (count - 1)):
        low, high = edge_rows(block)
        return rows_gather(value), low, high
    me = lax.axis_index("rows")
    even = me % 2 == 0
    slots = jnp.zeros((count,) + value.shape, value.dtype)
    slots = lax.dynamic_update_index_in_dim(slots, value, me, 0)
    filled = (jnp.arange(count) == me).astype(value.dtype)
    first, last = block[:, :, :1], block[:, :, -1:]
    shifted = [(i, (i + 1) % count) for i in range(1, count, 2)]
    shifted += [((i + 1) % count, i) for i in range(1, count, 2)]
    rounds = [([(i, i ^ 1) for i in range(count)], jnp.where(even, last, first))]
    rounds.append((shifted, jnp.where(even, first, last)))
    mask = 4
    while mask < count:
        rounds.append(([(i, i ^ mask) for i in range(count)], None))
        mask *= 2
    edges = []
    for pairs, edge in rounds:
        parts = [slots.reshape(-1), filled] + ([] if edge is None else [edge.reshape(-1)])
        message = lax.ppermute(jnp.concatenate(parts), "rows", pairs)
        got_slots = message[: slots.size].reshape(slots.shape)
        got_filled = message[slots.size : slots.size + count]
        if edge is not None:
            edges.append(message[slots.size + count :].reshape(edge.shape))
        keep = got_filled.reshape((count,) + (1,) * value.ndim) > 0
        slots = jnp.where(keep, got_slots, slots)
        filled = jnp.maximum(filled, got_filled)
    low = jnp.where(even, edges[1], edges[0])
    high = jnp.where(even, edges[0], edges[1])
    return slots, low, high


def gather_patches(grown_rows):
    frames, padded_rows, columns, channels = grown_rows.shape
    inner_rows = padded_rows - 2
    padded = jnp.pad(grown_rows, ((1, 1), (0, 0), (1, 1), (0, 0)))
    pieces = []
    for lag_frame in range(3):
        for lag_row in range(3):
            for lag_column in range(3):
                pieces.append(
                    padded[
                        lag_frame : lag_frame + frames,
                        lag_row : lag_row + inner_rows,
                        lag_column : lag_column + columns,
                        :,
                    ]
                )
    return jnp.concatenate(pieces, axis=-1).reshape(frames * inner_rows * columns, 27 * channels)


def conv_rows(grown, weights):
    batches, frames, grown_rows, columns, _ = grown.shape
    patches = jax.vmap(gather_patches)(grown).reshape(-1, weights.shape[0])
    out = jnp.dot(patches, weights, preferred_element_type=jnp.float32)
    return out.reshape(batches, frames, grown_rows - 2, columns, weights.shape[1])


def flipped(weights):
    channels = weights.shape[1]
    blocks = weights.reshape(27, -1, channels)[::-1]
    return jnp.swapaxes(blocks, 1, 2).reshape(-1, blocks.shape[1])


def with_halo(low, own, high, keep_low, keep_high):
    low = jnp.where(keep_low, low, jnp.zeros_like(low))
    high = jnp.where(keep_high, high, jnp.zeros_like(high))
    return jnp.concatenate([low, own, high], axis=2)


def forward_block(volume, gain_vec, weights, counted, keep_low, keep_high):
    batches = volume.shape[0]
    channels = volume.shape[-1]
    local_count = counted // lax.axis_size("rows")
    grouped = volume.reshape(batches, -1, GROUPS, channels // GROUPS)
    local_sum = jnp.sum(grouped, axis=(1, 3))
    local_mean = local_sum / local_count
    deviation = grouped - local_mean[:, None, :, None]
    local_sq = jnp.sum(deviation * deviation, axis=(1, 3))
    gathered, low, high = gather_with_halo(jnp.stack([local_sum, local_sq]), volume)
    sums = gathered[:, 0]
    squares = gathered[:, 1]
    centre = jnp.sum(sums, axis=0) / counted
    part_means = sums / local_count
    spread = (
        jnp.sum(squares, axis=0) + local_count * jnp.sum((part_means - centre) ** 2, axis=0)
    ) / counted
    inverse = lax.rsqrt(spread + EPSILON)
    full = jnp.concatenate([low, volume, high], axis=2)
    normed = (full - spread_groups(centre, channels)) * spread_groups(inverse, channels)
    active = jax.nn.silu(normed * gain_vec).astype(jnp.bfloat16)
    active = with_halo(active[:, :, :1], active[:, :, 1:-1], active[:, :, -1:], keep_low, keep_high)
    result = volume + conv_rows(active, weights)
    return active, centre, inverse, result


def backward_block(volume, gain_vec, reverse_weights, centre, inverse, cot, counted, keep_low, keep_high):
    channels = volume.shape[-1]
    batches = volume.shape[0]
    inverse_full = spread_groups(inverse, channels)
    normed = (volume - spread_groups(centre, channels)) * inverse_full
    zvalue = normed * gain_vec
    cot_low = cot.astype(jnp.bfloat16)
    act_grad = conv_rows(cot_low, reverse_weights)
    logistic = jax.nn.sigmoid(zvalue)
    pre_grad = act_grad * logistic * (1.0 + zvalue * (1.0 - logistic))
    hat_grad = pre_grad * gain_vec
    grouped_grad = hat_grad.reshape(batches, -1, GROUPS, channels // GROUPS)
    grouped_hat = normed.reshape(batches, -1, GROUPS, channels // GROUPS)
    parts, halo_low, halo_high = gather_with_halo(
        jnp.stack([jnp.sum(grouped_grad, axis=(1, 3)), jnp.sum(grouped_grad * grouped_hat, axis=(1, 3))]),
        jnp.concatenate([hat_grad, normed], axis=-1),
    )
    sums = jnp.sum(parts, axis=0)
    first = spread_groups(sums[0] / counted, channels)
    second = spread_groups(sums[1] / counted, channels)
    grad_full = jnp.concatenate([halo_low[..., :channels], hat_grad, halo_high[..., :channels]], axis=2)
    hat_full = jnp.concatenate([halo_low[..., channels:], normed, halo_high[..., channels:]], axis=2)
    passed = cot + inverse_full * (grad_full - first - hat_full * second)
    passed = with_halo(passed[:, :, :1], passed[:, :, 1:-1], passed[:, :, -1:], keep_low, keep_high)
    gain_part = jnp.sum((pre_grad * normed).reshape(-1, channels), axis=0)
    return passed, cot_low[:, :, 1:-1], gain_part


def weight_gradient(grown, cot_low):
    patches = jax.vmap(gather_patches)(grown)
    patches = patches.reshape(-1, patches.shape[-1])
    flat_cot = cot_low.reshape(-1, cot_low.shape[-1])
    return lax.dot_general(
        patches, flat_cot, (((0,), (0,)), ((), ())), preferred_element_type=jnp.float32
    )


def halving_order(bits):
    order = [b for b in (0, 1, bits - 1) if 0 <= b < bits]
    order = list(dict.fromkeys(order))
    return order + [b for b in range(bits) if b not in order]


def tree_scatter(packed):
    row_count = lax.axis_size("rows")
    dp_count = lax.axis_size("dp")
    if (row_count & (row_count - 1)) or (dp_count & (dp_count - 1)):
        return lax.psum_scatter(packed, ("rows", "dp"), scatter_dimension=0, tiled=True)[0]
    row_bits = row_count.bit_length() - 1
    dp_bits = dp_count.bit_length() - 1
    names = [("rows", row_bits - 1 - k) for k in range(row_bits)]
    names += [("dp", dp_bits - 1 - k) for k in range(dp_bits)]
    buf = packed.reshape((2,) * (row_bits + dp_bits) + packed.shape[1:])
    steps = [("rows", b) for b in halving_order(row_bits)] + [("dp", b) for b in range(dp_bits)]
    for axis, bit in steps:
        place = names.index((axis, bit))
        mine = (lax.axis_index(axis) >> bit) & 1
        keep = lax.dynamic_index_in_dim(buf, mine, place, keepdims=False)
        send = lax.dynamic_index_in_dim(buf, 1 - mine, place, keepdims=False)
        count = lax.axis_size(axis)
        buf = keep + lax.ppermute(send, axis, [(i, i ^ (1 << bit)) for i in range(count)])
        names.pop(place)
    return buf


def reduced_grads(weight_grad, gain_grad):
    shards = lax.axis_size("rows") * lax.axis_size("dp")
    rows_out = weight_grad.shape[0] // shards
    gains_out = gain_grad.shape[0] // shards
    packed = jnp.concatenate(
        [weight_grad.reshape(shards, -1), gain_grad.reshape(shards, gains_out)], axis=1
    )
    total = tree_scatter(packed)
    split = rows_out * weight_grad.shape[1]
    return total[:split].reshape(rows_out, weight_grad.shape[1]), total[split:]


def section_gather(value):
    count = lax.axis_size("section")
    if count & (count - 1):
        return lax.all_gather(value, "section")
    slots = jnp.zeros((count,) + value.shape, value.dtype)
    slots = lax.dynamic_update_index_in_dim(slots, value, lax.axis_index("section"), 0)
    mask = 1
    while mask < count:
        slots = slots + lax.ppermute(slots, "section", [(i, i ^ mask) for i in range(count)])
        mask *= 2
    return slots


def section_weights(weights):
    rows_count = lax.axis_size("rows")
    half = weights.shape[0] // 2
    if rows_count % 2 or weights.shape[0] % 2:
        return lax.all_gather(weights, "section")
    core = lax.axis_index("rows") % 2
    mine = lax.all_gather(lax.dynamic_slice_in_dim(weights, core * half, half, 0), "section")
    other = lax.ppermute(mine, "rows", [(i, i ^ 1) for i in range(rows_count)])
    low = jnp.where(core == 0, mine, other)
    high = jnp.where(core == 0, other, mine)
    return jnp.concatenate([low, high], axis=1)


def on_device(latent, enc_weight, dec_weight, enc_gain, dec_gain, out_grad):
    section_pos = lax.axis_index("section")
    rows_pos = lax.axis_index("rows")
    keep_low = rows_pos > 0
    keep_high = rows_pos < lax.axis_size("rows") - 1
    batches, frames, rows_here, columns, channels = latent.shape
    levels = lax.axis_size("section")
    counted = frames * rows_here * columns * (channels // GROUPS) * lax.axis_size("rows")
    cells_all = batches * lax.axis_size("dp") * frames * rows_here * lax.axis_size("rows") * columns
    loss_scale = 1.0 / math.sqrt(cells_all)
    enc_all = section_weights(enc_weight[0])
    dec_all = section_weights(dec_weight[0])
    gains_all = section_gather(jnp.stack([enc_gain[0], dec_gain[0]]))
    enc_gains = gains_all[:, 0]
    dec_gains = gains_all[:, 1]

    hidden = latent.astype(jnp.float32)
    enc_inputs = []
    enc_active = []
    enc_stats = []
    for level in range(levels):
        enc_inputs.append(hidden)
        active, centre, inverse, result = forward_block(
            hidden, enc_gains[level], enc_all[level], counted, keep_low, keep_high
        )
        enc_active.append(active)
        enc_stats.append((centre, inverse))
        hidden = result.astype(jnp.bfloat16).astype(jnp.float32)
    dec_inputs = [None] * levels
    dec_active = [None] * levels
    dec_stats = [None] * levels
    coming = hidden
    for level in reversed(range(levels)):
        united = coming + enc_inputs[level]
        dec_inputs[level] = united
        active, centre, inverse, result = forward_block(
            united, dec_gains[level], dec_all[level], counted, keep_low, keep_high
        )
        dec_active[level] = active
        dec_stats[level] = (centre, inverse)
        coming = result.astype(jnp.bfloat16).astype(jnp.float32)

    seeded_low, seeded_high = edge_rows(out_grad)
    cot = with_halo(seeded_low, out_grad, seeded_high, keep_low, keep_high).astype(jnp.float32) * loss_scale
    skip_grads = [None] * levels
    dec_cots = [None] * levels
    dec_gain_parts = [None] * levels
    for level in range(levels):
        cot, cot_low, gain_part = backward_block(
            dec_inputs[level],
            dec_gains[level],
            flipped(dec_all[level]),
            dec_stats[level][0],
            dec_stats[level][1],
            cot,
            counted,
            keep_low,
            keep_high,
        )
        skip_grads[level] = cot
        dec_cots[level] = cot_low
        dec_gain_parts[level] = gain_part
    own_dec = weight_gradient(
        lax.dynamic_index_in_dim(jnp.stack(dec_active), section_pos, 0, keepdims=False),
        lax.dynamic_index_in_dim(jnp.stack(dec_cots), section_pos, 0, keepdims=False),
    )
    dec_gain_own = lax.dynamic_index_in_dim(jnp.stack(dec_gain_parts), section_pos, 0, keepdims=False)
    dec_result, dec_gains_out = reduced_grads(own_dec, dec_gain_own)

    enc_cots = [None] * levels
    enc_gain_parts = [None] * levels
    for level in reversed(range(levels)):
      passed, cot_low, gain_part = backward_block(
          enc_inputs[level],
          enc_gains[level],
          flipped(enc_all[level]),
          enc_stats[level][0],
          enc_stats[level][1],
          cot,
          counted,
          keep_low,
          keep_high,
      )
      cot = passed + skip_grads[level]
      enc_cots[level] = cot_low
      enc_gain_parts[level] = gain_part
    own_enc = weight_gradient(
        lax.dynamic_index_in_dim(jnp.stack(enc_active), section_pos, 0, keepdims=False),
        lax.dynamic_index_in_dim(jnp.stack(enc_cots), section_pos, 0, keepdims=False),
    )
    enc_gain_own = lax.dynamic_index_in_dim(jnp.stack(enc_gain_parts), section_pos, 0, keepdims=False)
    enc_result, enc_gains_out = reduced_grads(own_enc, enc_gain_own)
    return (enc_result[None], dec_result[None], enc_gains_out[None], dec_gains_out[None])


def solution(mesh):
    in_specs = (
        P("dp", None, "rows", None, None),
        P("section", None, None),
        P("section", None, None),
        P("section", None),
        P("section", None),
        P("dp", None, "rows", None, None),
    )
    out_specs = (
        P("section", ("rows", "dp"), None),
        P("section", ("rows", "dp"), None),
        P("section", ("rows", "dp")),
        P("section", ("rows", "dp")),
    )

    return jax.shard_map(on_device, mesh=mesh, in_specs=in_specs, out_specs=out_specs, check_vma=False)
```
